256 devices in a mesh: cent: 8 (over z), dp: 32 (over x, y, core).
Axes of the slice: x: 4, y: 4, z: 8, core: 2. Of those that a mesh axis runs over, the one named last changes fastest.
Arguments:
- points: bfloat16 [32768, 1024], P('dp'), may hold values from -6 to 6
- cluster_ids: int32 [32768, 1], P('dp'), may hold values from 0 to 63; in each aligned block of 1024 rows (0 to 1023, 1024 to 2047, ...) at most 64 rows name the same one
- centroids: bfloat16 [8192, 1024], P('cent'), may hold values from -6 to 6
- sub_centroids: bfloat16 [64, 1024, 1024], P('dp', 'cent'), may hold values from -6 to 6
Outputs:
- assign: bfloat16 [32768, 8192], P('dp', 'cent')
- sub_assign: bfloat16 [32768, 1024], P('dp', 'cent')
The draws below stay inside these ranges and needn't reach their ends.
Inputs may be any that keep to these rules, and one draw needn't show every extreme that they name: `cluster_ids`: among the 1024 points of one index of dp, no level-two cluster holds more than 64 points; some cluster holds exactly 64 in some block.
All inputs are finite; a program needn't handle non-finite values.
Results may differ from the reference program's by a relative error of at most 0.001.
Values may be sent and summed in bfloat16 or wider, within the bound.
No kernel may reach another device: no remote copies, remote signals or barrier semaphores. Data moves between devices by JAX's collectives and lax.ppermute only.
A program may use at most 128 MiB of HBM per device.

```python
import math
import jax
import jax.numpy as jnp
import numpy as np
from jax import lax

D = 1024
K_DEV = 1024
CAP = 64
ITERS = 3
PTS_DEV = 1024
POINTS = 32768
K = 8192
SUB = 1024
L2 = 64


def shared_direction(key):
    base = jax.random.fold_in(key, 11)
    return jnp.clip(jax.random.normal(base, (D,), jnp.float32), -3.0, 3.0)


def loadings(key, rows, block, tag):
    blocks = rows // block
    base = jax.random.fold_in(key, tag)
    means = jax.random.uniform(jax.random.fold_in(base, 1), (blocks, 1), jnp.float32, -0.3, 0.3)
    jitter = jax.random.uniform(jax.random.fold_in(base, 2), (blocks, block), jnp.float32, -0.2, 0.2)
    return (means + jitter).reshape(rows)


def noisy_rows(key, rows, tag):
    base = jax.random.fold_in(key, tag)
    return jnp.clip(jax.random.normal(base, (rows, D), jnp.float32), -3.0, 3.0)


def draw_points(key, part):
    direction = shared_direction(key)
    loading = loadings(key, POINTS, PTS_DEV, 21)
    values = noisy_rows(key, POINTS, 31) + loading[:, None] * direction[None, :]
    return jnp.clip(values, -6.0, 6.0).astype(jnp.bfloat16)


def draw_centroids(key, part):
    direction = shared_direction(key)
    loading = loadings(key, K, K_DEV, 22)
    values = noisy_rows(key, K, 32) + loading[:, None] * direction[None, :]
    return jnp.clip(values, -6.0, 6.0).astype(jnp.bfloat16)


def steps_of(own_key, shape, shards, low, largest):
    factor_of = 1.0
    for position, blocks in shards:
        steps = jax.random.uniform(jax.random.fold_in(jax.random.fold_in(own_key, 6), position), (blocks,), jnp.float32, low / len(shards), largest / len(shards))
        factor_of = factor_of * jnp.repeat(jnp.exp(steps), shape[position] // blocks).reshape((-1,) + (1,) * (len(shape) - 1 - position))
    return factor_of


def routed_block(stream_key, own, number, rows, count, top, bound, lean):
    order = jax.random.permutation(stream_key, count)
    heavy_load, usual = portions_of(count, rows * top, bound, lean, True), portions_of(count, rows * top, bound, lean, False)
    places = jnp.arange(count)

    def named(sizes, rotation):
        used = int((sizes > 0).sum())
        fixed = max(1, used // 4)
        shifted = fixed + (places - fixed + rotation * (used - fixed)) % max(1, count - fixed)
        return jnp.zeros((count,), jnp.int32).at[order[jnp.where(places < fixed, places, shifted)]].set(jnp.asarray(sizes, jnp.int32))

    sizes = jnp.where(number % 4 == 0, named(heavy_load, number // 4), named(usual, number - number // 4 - 1))
    mixed = jax.random.permutation(jax.random.fold_in(own, 3), count)
    donor, sink = mixed[0:count // 2 * 2:2], mixed[1:count // 2 * 2:2]
    room = jnp.minimum(sizes[donor] - 1, bound - sizes[sink]) // 2
    room = jnp.where((donor == order[0]) | (sink == order[0]) | (sizes[sink] == 0), 0, jnp.maximum(room, 0))
    shifted = jax.random.randint(jax.random.fold_in(own, 4), (count // 2,), 0, 1 << 20) % (room + 1)
    sizes = sizes.at[donor].add(-shifted).at[sink].add(shifted)
    members = jnp.searchsorted(jnp.cumsum(sizes), jnp.arange(rows * top), side="right").astype(jnp.int32)
    table = members.reshape(top, rows).T
    table = table[jax.random.permutation(jax.random.fold_in(own, 1), rows)]
    rotation = jax.random.randint(jax.random.fold_in(own, 2), (rows, 1), 0, top)
    return jnp.take_along_axis(table, (jnp.arange(top)[None, :] + rotation) % top, axis=1)


def portions_of(amount, total, limit, skew, full):
    loads = [(1 << 20) // math.isqrt(standing ** skew) + 1 for standing in range(1, amount + 1)]
    largest = limit if full else min(limit, max(-(-total // amount), total * loads[0] // sum(loads)))
    least = 1 if total - largest >= amount - 1 else 0
    given, surplus = [largest] + [least] * (amount - 1), total - largest - least * (amount - 1)
    while surplus > 0:
        movable = [i for i in range(1, amount) if given[i] < largest] or [i for i in range(1, amount) if given[i] < limit]
        pool, budget = sum([loads[i] for i in movable]), surplus
        for i in movable:
            more = min(limit - given[i], max(1, budget * loads[i] // pool), surplus)
            given[i] = given[i] + more
            surplus = surplus - more
    return np.array(given)


def noise(rng, extent, spread, limit, shards=(), kind=jnp.bfloat16):
    result = jax.random.normal(rng, extent, jnp.float32) * spread
    if len(shards) > 0:
        result = steps_of(rng, extent, shards, -0.22, 0.18) * result
    return jnp.clip(result, min=-limit, max=limit).astype(kind)


def setup_inputs(seed: int = 0) -> dict:
    keys = jax.random.split(jax.random.key(seed), 5)
    points = draw_points(jax.random.fold_in(keys[4], 71), 0)
    cluster_ids_keys = jax.random.split(jax.random.fold_in(keys[1], 1), POINTS // PTS_DEV)
    cluster_ids_turns = jax.random.permutation(jax.random.fold_in(keys[1], 3), POINTS // PTS_DEV)
    cluster_ids = jax.vmap(lambda own, number: routed_block(jax.random.fold_in(keys[1], 2), own, number, PTS_DEV, L2, 1, CAP, 2))(cluster_ids_keys, cluster_ids_turns).reshape((POINTS, 1))
    centroids = draw_centroids(jax.random.fold_in(keys[4], 71), 0)
    sub_centroids = noise(keys[3], (L2, SUB, D), 1.0, 6.0, ((0, 32), (1, 8)))
    return {"points": points, "cluster_ids": cluster_ids, "centroids": centroids, "sub_centroids": sub_centroids}


EPS = 1e-06
TAU = 0.05

def inverse_norm(rows):
    values = rows.astype(jnp.float32)
    return lax.rsqrt(lax.optimization_barrier(jnp.mean(values * values, axis=-1)) + EPS)

def reference(points, cluster_ids, centroids, sub_centroids):
    width = points.shape[1]
    inv_x = inverse_norm(points)
    inv_c = inverse_norm(centroids)
    inv_u = inverse_norm(sub_centroids)
    scores = jnp.dot(points, centroids.T, preferred_element_type=jnp.float32)
    expo = jnp.exp(scores * inv_x[:, None] * inv_c[None, :] * (1.0 / (width * TAU)))
    row_scale = jnp.ones((points.shape[0],), jnp.float32)
    col_scale = jnp.ones((centroids.shape[0],), jnp.float32)
    for step in range(ITERS):
        col_scale = 1.0 / jnp.dot(row_scale, expo, precision=lax.Precision.HIGHEST)
        row_scale = 1.0 / jnp.dot(expo, col_scale, precision=lax.Precision.HIGHEST)
    assign = (expo * row_scale[:, None] * col_scale[None, :] * K).astype(jnp.bfloat16)
    block = 16
    ids = cluster_ids[:, 0].astype(jnp.int32)
    point_blocks = points.reshape(-1, block, width)
    id_blocks = ids.reshape(-1, block)
    inv_blocks = inv_x.reshape(-1, block)

    def level_two(item):
        rows, labels, inv_rows = item
        chosen = sub_centroids[labels].astype(jnp.float32)
        dots = jnp.einsum('bd,bsd->bs', rows.astype(jnp.float32), chosen)
        weights = jnp.exp(dots * inv_rows[:, None] * inv_u[labels] * (1.0 / (width * TAU)))
        return SUB * weights / lax.optimization_barrier(jnp.sum(weights, axis=1, keepdims=True))
    sub_assign = lax.map(level_two, (point_blocks, id_blocks, inv_blocks))
    sub_assign = sub_assign.reshape(points.shape[0], SUB).astype(jnp.bfloat16)
    return (assign, sub_assign)
```

```python
import jax
import jax.numpy as jnp
from jax import lax
from jax.sharding import PartitionSpec as P

CAP = 64
ITERS = 3


EPS = 1e-06
TAU = 0.05


def inverse_norm(rows):
    values = rows.astype(jnp.float32)
    return lax.rsqrt(jnp.mean(values * values, axis=-1) + EPS)


def shards(points, cluster_ids, centroids, sub_centroids):
    pts_count = points.shape[0]
    width = points.shape[1]
    dp_count = lax.axis_size("dp")
    cent_count = lax.axis_size("cent")
    group_dev = sub_centroids.shape[0]
    sub_dev = sub_centroids.shape[1]
    clusters = group_dev * dp_count
    total_cent = centroids.shape[0] * cent_count
    total_sub = sub_dev * cent_count
    scale_two = 1.0 / (width * TAU)

    ids = cluster_ids[:, 0]
    labels = lax.broadcasted_iota(jnp.int32, (pts_count, clusters), 1)
    onehot = ids[:, None] == labels
    positions = lax.broadcasted_iota(jnp.int32, (pts_count, pts_count), 0)
    earlier = (positions > positions.T).astype(jnp.bfloat16)
    before = jnp.dot(earlier, onehot.astype(jnp.bfloat16), preferred_element_type=jnp.float32)
    rank = jnp.sum(before * onehot.astype(jnp.float32), axis=1).astype(jnp.int32)
    slot = ids * CAP + rank
    buffer = jnp.zeros((clusters * CAP, width), jnp.bfloat16).at[slot].set(points)
    outgoing = buffer.reshape(dp_count, group_dev * CAP, width)
    arrived = lax.all_to_all(outgoing, "dp", split_axis=0, concat_axis=0, tiled=True)
    arrived = arrived.reshape(dp_count, group_dev, CAP, width)
    inv_u = inverse_norm(sub_centroids)
    inv_rows = inverse_norm(arrived)
    dots = jnp.einsum("sgcd,gkd->sgck", arrived, sub_centroids, preferred_element_type=jnp.float32)
    weights = jnp.exp(dots * inv_rows[..., None] * inv_u[None, :, None, :] * scale_two)
    weights = weights.reshape(dp_count, group_dev * CAP, sub_dev)
    returned = lax.all_to_all(weights, "dp", split_axis=0, concat_axis=0, tiled=True)

    inv_x = inverse_norm(points)
    inv_c = inverse_norm(centroids)
    scores = jnp.einsum("pd,kd->pk", points, centroids, preferred_element_type=jnp.float32)
    expo = jnp.exp(scores * inv_x[:, None] * inv_c[None, :] * (1.0 / (width * TAU)))
    col_part = jnp.sum(expo, axis=0)
    col_part, returned = lax.optimization_barrier((col_part, returned))
    row_part = None
    for step in range(ITERS):
        if step > 0:
            col_part = jnp.sum(expo * row_scale[:, None], axis=0)
        col_scale = 1.0 / lax.psum(col_part, "dp")
        row_part = jnp.sum(expo * col_scale[None, :], axis=1)
        if step + 1 < ITERS:
            row_scale = 1.0 / lax.psum(row_part, "cent")

    slot_weights = returned.reshape(clusters * CAP, sub_dev)
    point_weights = slot_weights[slot]
    denom_part = jnp.sum(point_weights, axis=1)
    row_total = lax.psum(row_part, "cent")
    denominator = lax.psum(denom_part, "cent")
    row_scale = 1.0 / row_total
    assign = (expo * row_scale[:, None] * col_scale[None, :] * total_cent).astype(jnp.bfloat16)
    sub_assign = (total_sub * point_weights / denominator[:, None]).astype(jnp.bfloat16)
    return (assign, sub_assign)


def solution(mesh):
    return jax.shard_map(
        shards,
        mesh=mesh,
        in_specs=(P("dp", None), P("dp", None), P("cent", None), P("dp", "cent", None)),
        out_specs=(P("dp", "cent"), P("dp", "cent")),
        check_vma=False,
    )
```

```python
import jax
import jax.numpy as jnp
from jax import lax
from jax.sharding import PartitionSpec as P

CAP = 64
ITERS = 3


EPS = 1e-06
TAU = 0.05


def inverse_norm(rows):
    values = rows.astype(jnp.float32)
    return lax.rsqrt(jnp.mean(values * values, axis=-1) + EPS)


def shift_pairs(count, stride, size, step):
    pairs = []
    for i in range(count):
        digit = (i // stride) % size
        pairs.append((i, i + (((digit + step) % size) - digit) * stride))
    return pairs


def dp_sum(values):
    count = lax.axis_size("dp")
    for stride, size in ((1, 2), (2, 4), (8, count // 8)):
        if size < 2:
            continue
        parts = [lax.ppermute(values, "dp", shift_pairs(count, stride, size, step)) for step in range(1, size)]
        for part in parts:
            values = values + part
    return values


def shards(points, cluster_ids, centroids, sub_centroids):
    pts_count = points.shape[0]
    width = points.shape[1]
    dp_count = lax.axis_size("dp")
    cent_count = lax.axis_size("cent")
    group_dev = sub_centroids.shape[0]
    sub_dev = sub_centroids.shape[1]
    clusters = group_dev * dp_count
    total_cent = centroids.shape[0] * cent_count
    total_sub = sub_dev * cent_count
    scale_two = 1.0 / (width * TAU)

    gathered = lax.all_gather(sub_centroids, "dp", axis=0, tiled=True)
    inv_x = inverse_norm(points)
    ids = cluster_ids[:, 0]
    labels = lax.broadcasted_iota(jnp.int32, (pts_count, clusters), 1)
    onehot = ids[:, None] == labels
    positions = lax.broadcasted_iota(jnp.int32, (pts_count, pts_count), 0)
    earlier = (positions > positions.T).astype(jnp.bfloat16)
    before = jnp.dot(earlier, onehot.astype(jnp.bfloat16), preferred_element_type=jnp.float32)
    rank = jnp.sum(before * onehot.astype(jnp.float32), axis=1).astype(jnp.int32)
    slot = ids * CAP + rank
    source = jnp.zeros((clusters * CAP,), jnp.int32).at[slot].set(jnp.arange(pts_count, dtype=jnp.int32))
    buffer = points[source].reshape(clusters, CAP, width)
    inv_rows = inv_x[source].reshape(clusters, CAP)
    inv_u = inverse_norm(gathered)
    dots = jnp.einsum("gcd,gkd->gck", buffer, gathered, preferred_element_type=jnp.float32)
    weights = jnp.exp(dots * inv_rows[..., None] * inv_u[:, None, :] * scale_two)
    point_weights = weights.reshape(clusters * CAP, sub_dev)[slot]
    denom_part = jnp.sum(point_weights, axis=1)

    inv_c = inverse_norm(centroids)
    scores = jnp.einsum("pd,kd->pk", points, centroids, preferred_element_type=jnp.float32)
    expo = jnp.exp(scores * inv_x[:, None] * inv_c[None, :] * (1.0 / (width * TAU)))
    row_part = None
    for step in range(ITERS):
        if step == 0:
            col_part = jnp.sum(expo, axis=0)
        else:
            col_part = jnp.sum(expo * row_scale[:, None], axis=0)
        col_scale = 1.0 / dp_sum(col_part)
        row_part = jnp.sum(expo * col_scale[None, :], axis=1)
        if step + 1 < ITERS:
            row_scale = 1.0 / lax.psum(row_part, "cent")

    row_total = lax.psum(row_part, "cent")
    denominator = lax.psum(denom_part, "cent")
    row_scale = 1.0 / row_total
    assign = (expo * row_scale[:, None] * col_scale[None, :] * total_cent).astype(jnp.bfloat16)
    sub_assign = (total_sub * point_weights / denominator[:, None]).astype(jnp.bfloat16)
    return (assign, sub_assign)


def solution(mesh):
    return jax.shard_map(
        shards,
        mesh=mesh,
        in_specs=(P("dp", None), P("dp", None), P("cent", None), P("dp", "cent", None)),
        out_specs=(P("dp", "cent"), P("dp", "cent")),
        check_vma=False,
    )
```

```python
import jax
import jax.numpy as jnp
from jax import lax
from jax.sharding import PartitionSpec as P

CAP = 64
ITERS = 3


EPS = 1e-06
TAU = 0.05


def inverse_norm(rows):
    values = rows.astype(jnp.float32)
    return lax.rsqrt(jnp.mean(values * values, axis=-1) + EPS)


def shift_pairs(count, stride, size, step):
    pairs = []
    for i in range(count):
        digit = (i // stride) % size
        pairs.append((i, i + (((digit + step) % size) - digit) * stride))
    return pairs


def dp_sum(values):
    count = lax.axis_size("dp")
    for stride, size in ((1, 2), (2, 4), (8, count // 8)):
        if size < 2:
            continue
        parts = [lax.ppermute(values, "dp", shift_pairs(count, stride, size, step)) for step in range(1, size)]
        for part in parts:
            values = values + part
    return values


def cent_sum(values):
    count = lax.axis_size("cent")
    bit = 1
    while bit < count:
        values = values + lax.ppermute(values, "cent", [(i, i ^ bit) for i in range(count)])
        bit *= 2
    return values


def shards(points, cluster_ids, centroids, sub_centroids):
    pts_count = points.shape[0]
    width = points.shape[1]
    dp_count = lax.axis_size("dp")
    cent_count = lax.axis_size("cent")
    group_dev = sub_centroids.shape[0]
    sub_dev = sub_centroids.shape[1]
    clusters = group_dev * dp_count
    total_cent = centroids.shape[0] * cent_count
    total_sub = sub_dev * cent_count
    scale_two = 1.0 / (width * TAU)

    gathered = lax.all_gather(sub_centroids, "dp", axis=0, tiled=True)
    inv_x = inverse_norm(points)
    ids = cluster_ids[:, 0]
    labels = lax.broadcasted_iota(jnp.int32, (pts_count, clusters), 1)
    onehot = ids[:, None] == labels
    positions = lax.broadcasted_iota(jnp.int32, (pts_count, pts_count), 0)
    earlier = (positions > positions.T).astype(jnp.bfloat16)
    before = jnp.dot(earlier, onehot.astype(jnp.bfloat16), preferred_element_type=jnp.float32)
    rank = jnp.sum(before * onehot.astype(jnp.float32), axis=1).astype(jnp.int32)
    slot = ids * CAP + rank
    source = jnp.zeros((clusters * CAP,), jnp.int32).at[slot].set(jnp.arange(pts_count, dtype=jnp.int32))
    pick = (source[:, None] == lax.broadcasted_iota(jnp.int32, (clusters * CAP, pts_count), 1)).astype(points.dtype)
    buffer = jnp.dot(pick, points, preferred_element_type=jnp.float32).astype(points.dtype)
    buffer = buffer.reshape(clusters, CAP, width)
    inv_rows = inverse_norm(buffer)
    inv_u = inverse_norm(gathered)
    dots = jnp.einsum("gcd,gkd->gck", buffer, gathered, preferred_element_type=jnp.float32)
    weights = jnp.exp(dots * inv_rows[..., None] * inv_u[:, None, :] * scale_two)
    point_weights = weights.reshape(clusters * CAP, sub_dev)[slot]
    denom_part = jnp.sum(point_weights, axis=1)

    inv_c = inverse_norm(centroids)
    scores = jnp.einsum("pd,kd->pk", points, centroids, preferred_element_type=jnp.float32)
    expo = jnp.exp(scores * inv_x[:, None] * inv_c[None, :] * (1.0 / (width * TAU)))
    row_part = None
    for step in range(ITERS):
        if step == 0:
            col_part = jnp.sum(expo, axis=0)
        else:
            col_part = jnp.sum(expo * row_scale[:, None], axis=0)
        col_scale = 1.0 / dp_sum(col_part)
        row_part = jnp.sum(expo * col_scale[None, :], axis=1)
        if step + 1 < ITERS:
            row_scale = 1.0 / cent_sum(row_part)

    totals = cent_sum(jnp.concatenate([row_part, denom_part]))
    row_total = totals[:pts_count]
    denominator = totals[pts_count:]
    row_scale = 1.0 / row_total
    assign = (expo * row_scale[:, None] * col_scale[None, :] * total_cent).astype(jnp.bfloat16)
    sub_assign = (total_sub * point_weights / denominator[:, None]).astype(jnp.bfloat16)
    return (assign, sub_assign)


def solution(mesh):
    return jax.shard_map(
        shards,
        mesh=mesh,
        in_specs=(P("dp", None), P("dp", None), P("cent", None), P("dp", "cent", None)),
        out_specs=(P("dp", "cent"), P("dp", "cent")),
        check_vma=False,
    )
```

```python
import jax
import jax.numpy as jnp
from jax import lax
from jax.sharding import PartitionSpec as P

CAP = 64
ITERS = 3


EPS = 1e-06
TAU = 0.05


def inverse_norm(rows):
    values = rows.astype(jnp.float32)
    return lax.rsqrt(jnp.mean(values * values, axis=-1) + EPS)


def shift_pairs(count, stride, size, step):
    pairs = []
    for i in range(count):
        digit = (i // stride) % size
        pairs.append((i, i + (((digit + step) % size) - digit) * stride))
    return pairs


def dp_sum(values):
    count = lax.axis_size("dp")
    for stride, size in ((1, 2), (2, 4), (8, count // 8)):
        if size < 2:
            continue
        parts = [lax.ppermute(values, "dp", shift_pairs(count, stride, size, step)) for step in range(1, size)]
        for part in parts:
            values = values + part
    return values


def cent_sum(values):
    count = lax.axis_size("cent")
    bit = 1
    while bit < count:
        values = values + lax.ppermute(values, "cent", [(i, i ^ bit) for i in range(count)])
        bit *= 2
    return values


def shards(points, cluster_ids, centroids, sub_centroids):
    pts_count = points.shape[0]
    width = points.shape[1]
    dp_count = lax.axis_size("dp")
    cent_count = lax.axis_size("cent")
    group_dev = sub_centroids.shape[0]
    sub_dev = sub_centroids.shape[1]
    clusters = group_dev * dp_count
    total_cent = centroids.shape[0] * cent_count
    total_sub = sub_dev * cent_count
    scale_two = 1.0 / (width * TAU)

    gathered = lax.all_gather(sub_centroids, "dp", axis=0, tiled=True)
    inv_x = inverse_norm(points)
    ids = cluster_ids[:, 0]
    labels = lax.broadcasted_iota(jnp.int32, (pts_count, clusters), 1)
    onehot = ids[:, None] == labels
    positions = lax.broadcasted_iota(jnp.int32, (pts_count, pts_count), 0)
    earlier = (positions > positions.T).astype(jnp.bfloat16)
    before = jnp.dot(earlier, onehot.astype(jnp.bfloat16), preferred_element_type=jnp.float32)
    rank = jnp.sum(before * onehot.astype(jnp.float32), axis=1).astype(jnp.int32)
    slot = ids * CAP + rank
    source = jnp.zeros((clusters * CAP,), jnp.int32).at[slot].set(jnp.arange(pts_count, dtype=jnp.int32))
    pick = (source[:, None] == lax.broadcasted_iota(jnp.int32, (clusters * CAP, pts_count), 1)).astype(points.dtype)
    buffer = jnp.dot(pick, points, preferred_element_type=jnp.float32).astype(points.dtype)
    buffer = buffer.reshape(clusters, CAP, width)
    inv_rows = inverse_norm(buffer)
    inv_u = inverse_norm(gathered)
    dots = jnp.einsum("gcd,gkd->gck", buffer, gathered, preferred_element_type=jnp.float32)
    weights = jnp.exp(dots * inv_rows[..., None] * inv_u[:, None, :] * scale_two)
    point_weights = weights.reshape(clusters * CAP, sub_dev)[slot]
    denom_part = jnp.sum(point_weights, axis=1)

    inv_c = inverse_norm(centroids)
    scores = jnp.einsum("pd,kd->pk", points, centroids, preferred_element_type=jnp.float32)
    expo = jnp.exp(scores * inv_x[:, None] * inv_c[None, :] * (1.0 / (width * TAU)))
    row_part = None
    for step in range(ITERS):
        if step == 0:
            col_part = jnp.sum(expo, axis=0)
        else:
            col_part = jnp.sum(expo * row_scale[:, None], axis=0)
        col_scale = 1.0 / dp_sum(col_part)
        row_part = jnp.sum(expo * col_scale[None, :], axis=1)
        if step + 1 < ITERS:
            row_scale = 1.0 / cent_sum(row_part)

    row_total = cent_sum(row_part)
    denominator = cent_sum(denom_part)
    row_scale = 1.0 / row_total
    assign = (expo * row_scale[:, None] * col_scale[None, :] * total_cent).astype(jnp.bfloat16)
    sub_assign = (total_sub * point_weights / denominator[:, None]).astype(jnp.bfloat16)
    return (assign, sub_assign)


def solution(mesh):
    return jax.shard_map(
        shards,
        mesh=mesh,
        in_specs=(P("dp", None), P("dp", None), P("cent", None), P("dp", "cent", None)),
        out_specs=(P("dp", "cent"), P("dp", "cent")),
        check_vma=False,
    )
```

```python
import jax
import jax.numpy as jnp
from jax import lax
from jax.experimental import pallas as pl
from jax.sharding import PartitionSpec as P

CAP = 64
ITERS = 3


EPS = 1e-06
TAU = 0.05
BLOCK = 8


def level_two_kernel(rows_ref, subs_ref, out_ref):
    width = rows_ref.shape[-1]
    scale = 1.0 / (width * TAU)
    ones = jnp.ones((8, width), jnp.bfloat16)
    nt = (((1,), (1,)), ((), ()))
    for g in range(rows_ref.shape[0]):
        rows = rows_ref[g]
        subs = subs_ref[g]
        wide = rows.astype(jnp.float32)
        inv_rows = lax.rsqrt(jnp.sum(wide * wide, axis=-1, keepdims=True) / width + EPS)
        square = subs.astype(jnp.float32) * subs.astype(jnp.float32)
        high = square.astype(jnp.bfloat16)
        low = (square - high.astype(jnp.float32)).astype(jnp.bfloat16)
        total = lax.dot_general(ones, high, nt, preferred_element_type=jnp.float32)
        total = total + lax.dot_general(ones, low, nt, preferred_element_type=jnp.float32)
        inv_u = lax.rsqrt(total[0:1, :] / width + EPS)
        dots = lax.dot_general(rows, subs, nt, preferred_element_type=jnp.float32)
        out_ref[g] = jnp.exp(dots * inv_rows * inv_u * scale)

def level_two(rows, subs):
    groups, cap, width = rows.shape
    count = subs.shape[1]
    return pl.pallas_call(
        level_two_kernel,
        grid=(groups // BLOCK,),
        in_specs=[pl.BlockSpec((BLOCK, cap, width), lambda i: (i, 0, 0)),
                  pl.BlockSpec((BLOCK, count, width), lambda i: (i, 0, 0))],
        out_specs=pl.BlockSpec((BLOCK, cap, count), lambda i: (i, 0, 0)),
        out_shape=jax.ShapeDtypeStruct((groups, cap, count), jnp.float32),
    )(rows, subs)


def inverse_norm(rows):
    values = rows.astype(jnp.float32)
    return lax.rsqrt(jnp.mean(values * values, axis=-1) + EPS)


def shift_pairs(count, stride, size, step):
    pairs = []
    for i in range(count):
        digit = (i // stride) % size
        pairs.append((i, i + (((digit + step) % size) - digit) * stride))
    return pairs


def dp_sum(values):
    count = lax.axis_size("dp")
    for stride, size in ((1, 2), (2, 4), (8, count // 8)):
        if size < 2:
            continue
        parts = [lax.ppermute(values, "dp", shift_pairs(count, stride, size, step)) for step in range(1, size)]
        for part in parts:
            values = values + part
    return values


def cent_sum(values):
    count = lax.axis_size("cent")
    bit = 1
    while bit < count:
        values = values + lax.ppermute(values, "cent", [(i, i ^ bit) for i in range(count)])
        bit *= 2
    return values


def shards(points, cluster_ids, centroids, sub_centroids):
    pts_count = points.shape[0]
    width = points.shape[1]
    dp_count = lax.axis_size("dp")
    cent_count = lax.axis_size("cent")
    group_dev = sub_centroids.shape[0]
    sub_dev = sub_centroids.shape[1]
    clusters = group_dev * dp_count
    total_cent = centroids.shape[0] * cent_count
    total_sub = sub_dev * cent_count
    scale_two = 1.0 / (width * TAU)

    gathered = lax.all_gather(sub_centroids, "dp", axis=0, tiled=True)
    inv_x = inverse_norm(points)
    ids = cluster_ids[:, 0]
    labels = lax.broadcasted_iota(jnp.int32, (pts_count, clusters), 1)
    onehot = ids[:, None] == labels
    positions = lax.broadcasted_iota(jnp.int32, (pts_count, pts_count), 0)
    earlier = (positions > positions.T).astype(jnp.bfloat16)
    before = jnp.dot(earlier, onehot.astype(jnp.bfloat16), preferred_element_type=jnp.float32)
    rank = jnp.sum(before * onehot.astype(jnp.float32), axis=1).astype(jnp.int32)
    slot = ids * CAP + rank
    source = jnp.zeros((clusters * CAP,), jnp.int32).at[slot].set(jnp.arange(pts_count, dtype=jnp.int32))
    pick = (source[:, None] == lax.broadcasted_iota(jnp.int32, (clusters * CAP, pts_count), 1)).astype(points.dtype)
    buffer = jnp.dot(pick, points, preferred_element_type=jnp.float32).astype(points.dtype)
    buffer = buffer.reshape(clusters, CAP, width)
    weights = level_two(buffer, gathered)
    point_weights = weights.reshape(clusters * CAP, sub_dev)[slot]
    denom_part = jnp.sum(point_weights, axis=1)

    inv_c = inverse_norm(centroids)
    scores = jnp.einsum("pd,kd->pk", points, centroids, preferred_element_type=jnp.float32)
    expo = jnp.exp(scores * inv_x[:, None] * inv_c[None, :] * (1.0 / (width * TAU)))
    row_part = None
    for step in range(ITERS):
        if step == 0:
            col_part = jnp.sum(expo, axis=0)
        else:
            col_part = jnp.sum(expo * row_scale[:, None], axis=0)
        col_scale = 1.0 / dp_sum(col_part)
        row_part = jnp.sum(expo * col_scale[None, :], axis=1)
        if step + 1 < ITERS:
            row_scale = 1.0 / cent_sum(row_part)

    row_total = cent_sum(row_part)
    denominator = cent_sum(denom_part)
    row_scale = 1.0 / row_total
    assign = (expo * row_scale[:, None] * col_scale[None, :] * total_cent).astype(jnp.bfloat16)
    sub_assign = (total_sub * point_weights / denominator[:, None]).astype(jnp.bfloat16)
    return (assign, sub_assign)


def solution(mesh):
    return jax.shard_map(
        shards,
        mesh=mesh,
        in_specs=(P("dp", None), P("dp", None), P("cent", None), P("dp", "cent", None)),
        out_specs=(P("dp", "cent"), P("dp", "cent")),
        check_vma=False,
    )
```

```python
import jax
import jax.numpy as jnp
from jax import lax
from jax.sharding import PartitionSpec as P

CAP = 64
ITERS = 3


EPS = 1e-06
TAU = 0.05


def inverse_norm(rows):
    values = rows.astype(jnp.float32)
    return lax.rsqrt(jnp.mean(values * values, axis=-1) + EPS)


def shift_pairs(count, stride, size, step):
    pairs = []
    for i in range(count):
        digit = (i // stride) % size
        pairs.append((i, i + (((digit + step) % size) - digit) * stride))
    return pairs


def dp_sum(values):
    count = lax.axis_size("dp")
    for stride, size in ((1, 2), (2, 4), (8, count // 8)):
        if size < 2:
            continue
        parts = [lax.ppermute(values, "dp", shift_pairs(count, stride, size, step)) for step in range(1, size)]
        for part in parts:
            values = values + part
    return values


def cent_sum(values):
    count = lax.axis_size("cent")
    bit = 1
    while bit < count:
        values = values + lax.ppermute(values, "cent", [(i, i ^ bit) for i in range(count)])
        bit *= 2
    return values


def shards(points, cluster_ids, centroids, sub_centroids):
    pts_count = points.shape[0]
    width = points.shape[1]
    dp_count = lax.axis_size("dp")
    cent_count = lax.axis_size("cent")
    group_dev = sub_centroids.shape[0]
    sub_dev = sub_centroids.shape[1]
    clusters = group_dev * dp_count
    total_cent = centroids.shape[0] * cent_count
    total_sub = sub_dev * cent_count
    scale_two = 1.0 / (width * TAU)

    own_inv = inverse_norm(sub_centroids)
    spread = own_inv * 65537.0
    high = spread - (spread - own_inv)
    rest = own_inv - high
    spread = rest * 65537.0
    mid = spread - (spread - rest)
    low = (rest - mid).astype(jnp.bfloat16)
    high = high.astype(jnp.bfloat16)
    mid = mid.astype(jnp.bfloat16)
    extra = jnp.concatenate([high, mid, low, jnp.zeros((group_dev, width - 3 * sub_dev), jnp.bfloat16)], axis=1)
    pad = jnp.zeros((group_dev, 7, width), jnp.bfloat16)
    packed = jnp.concatenate([sub_centroids, extra[:, None, :], pad], axis=1)
    arrived = lax.all_gather(packed, "dp", axis=0, tiled=True)
    gathered = arrived[:, :sub_dev, :]
    parts = arrived[:, sub_dev, : 3 * sub_dev].astype(jnp.float32)
    inv_u = (parts[:, :sub_dev] + parts[:, sub_dev : 2 * sub_dev]) + parts[:, 2 * sub_dev :]
    inv_x = inverse_norm(points)
    ids = cluster_ids[:, 0]
    labels = lax.broadcasted_iota(jnp.int32, (pts_count, clusters), 1)
    onehot = ids[:, None] == labels
    positions = lax.broadcasted_iota(jnp.int32, (pts_count, pts_count), 0)
    earlier = (positions > positions.T).astype(jnp.bfloat16)
    before = jnp.dot(earlier, onehot.astype(jnp.bfloat16), preferred_element_type=jnp.float32)
    rank = jnp.sum(before * onehot.astype(jnp.float32), axis=1).astype(jnp.int32)
    slot = ids * CAP + rank
    source = jnp.zeros((clusters * CAP,), jnp.int32).at[slot].set(jnp.arange(pts_count, dtype=jnp.int32))
    pick = (source[:, None] == lax.broadcasted_iota(jnp.int32, (clusters * CAP, pts_count), 1)).astype(points.dtype)
    buffer = jnp.dot(pick, points, preferred_element_type=jnp.float32).astype(points.dtype)
    buffer = buffer.reshape(clusters, CAP, width)
    inv_rows = inverse_norm(buffer)
    dots = jnp.einsum("gcd,gkd->gck", buffer, gathered, preferred_element_type=jnp.float32)
    weights = jnp.exp(dots * inv_rows[..., None] * inv_u[:, None, :] * scale_two)
    point_weights = weights.reshape(clusters * CAP, sub_dev)[slot]
    denom_part = jnp.sum(point_weights, axis=1)

    inv_c = inverse_norm(centroids)
    scores = jnp.einsum("pd,kd->pk", points, centroids, preferred_element_type=jnp.float32)
    expo = jnp.exp(scores * inv_x[:, None] * inv_c[None, :] * (1.0 / (width * TAU)))
    row_part = None
    for step in range(ITERS):
        if step == 0:
            col_part = jnp.sum(expo, axis=0)
        else:
            col_part = jnp.sum(expo * row_scale[:, None], axis=0)
        col_scale = 1.0 / dp_sum(col_part)
        row_part = jnp.sum(expo * col_scale[None, :], axis=1)
        if step + 1 < ITERS:
            row_scale = 1.0 / cent_sum(row_part)

    row_total = cent_sum(row_part)
    denominator = cent_sum(denom_part)
    row_scale = 1.0 / row_total
    assign = (expo * row_scale[:, None] * col_scale[None, :] * total_cent).astype(jnp.bfloat16)
    sub_assign = (total_sub * point_weights / denominator[:, None]).astype(jnp.bfloat16)
    return (assign, sub_assign)


def solution(mesh):
    return jax.shard_map(
        shards,
        mesh=mesh,
        in_specs=(P("dp", None), P("dp", None), P("cent", None), P("dp", "cent", None)),
        out_specs=(P("dp", "cent"), P("dp", "cent")),
        check_vma=False,
    )
```

```python
import jax
import jax.numpy as jnp
from jax import lax
from jax.sharding import PartitionSpec as P

CAP = 64
ITERS = 3


EPS = 1e-06
TAU = 0.05


def inverse_norm(rows):
    values = rows.astype(jnp.float32)
    return lax.rsqrt(jnp.mean(values * values, axis=-1) + EPS)


def shift_pairs(count, stride, size, step):
    pairs = []
    for i in range(count):
        digit = (i // stride) % size
        pairs.append((i, i + (((digit + step) % size) - digit) * stride))
    return pairs


def dp_sum(values):
    count = lax.axis_size("dp")
    bit = 1
    while bit < count:
        values = values + lax.ppermute(values, "dp", [(i, i ^ bit) for i in range(count)])
        bit *= 2
    return values


def cent_sum(values):
    count = lax.axis_size("cent")
    bit = 1
    while bit < count:
        values = values + lax.ppermute(values, "cent", [(i, i ^ bit) for i in range(count)])
        bit *= 2
    return values


def shards(points, cluster_ids, centroids, sub_centroids):
    pts_count = points.shape[0]
    width = points.shape[1]
    dp_count = lax.axis_size("dp")
    cent_count = lax.axis_size("cent")
    group_dev = sub_centroids.shape[0]
    sub_dev = sub_centroids.shape[1]
    clusters = group_dev * dp_count
    total_cent = centroids.shape[0] * cent_count
    total_sub = sub_dev * cent_count
    scale_two = 1.0 / (width * TAU)

    own_inv = inverse_norm(sub_centroids)
    spread = own_inv * 65537.0
    high = spread - (spread - own_inv)
    rest = own_inv - high
    spread = rest * 65537.0
    mid = spread - (spread - rest)
    low = (rest - mid).astype(jnp.bfloat16)
    high = high.astype(jnp.bfloat16)
    mid = mid.astype(jnp.bfloat16)
    extra = jnp.concatenate([high, mid, low, jnp.zeros((group_dev, width - 3 * sub_dev), jnp.bfloat16)], axis=1)
    pad = jnp.zeros((group_dev, 7, width), jnp.bfloat16)
    packed = jnp.concatenate([sub_centroids, extra[:, None, :], pad], axis=1)
    arrived = lax.all_gather(packed, "dp", axis=0, tiled=True)
    gathered = arrived[:, :sub_dev, :]
    parts = arrived[:, sub_dev, : 3 * sub_dev].astype(jnp.float32)
    inv_u = (parts[:, :sub_dev] + parts[:, sub_dev : 2 * sub_dev]) + parts[:, 2 * sub_dev :]
    inv_x = inverse_norm(points)
    ids = cluster_ids[:, 0]
    labels = lax.broadcasted_iota(jnp.int32, (pts_count, clusters), 1)
    onehot = ids[:, None] == labels
    positions = lax.broadcasted_iota(jnp.int32, (pts_count, pts_count), 0)
    earlier = (positions > positions.T).astype(jnp.bfloat16)
    before = jnp.dot(earlier, onehot.astype(jnp.bfloat16), preferred_element_type=jnp.float32)
    rank = jnp.sum(before * onehot.astype(jnp.float32), axis=1).astype(jnp.int32)
    slot = ids * CAP + rank
    source = jnp.zeros((clusters * CAP,), jnp.int32).at[slot].set(jnp.arange(pts_count, dtype=jnp.int32))
    pick = (source[:, None] == lax.broadcasted_iota(jnp.int32, (clusters * CAP, pts_count), 1)).astype(points.dtype)
    buffer = jnp.dot(pick, points, preferred_element_type=jnp.float32).astype(points.dtype)
    buffer = buffer.reshape(clusters, CAP, width)
    inv_rows = inverse_norm(buffer)
    dots = jnp.einsum("gcd,gkd->gck", buffer, gathered, preferred_element_type=jnp.float32)
    weights = jnp.exp(dots * inv_rows[..., None] * inv_u[:, None, :] * scale_two)
    point_weights = weights.reshape(clusters * CAP, sub_dev)[slot]
    denom_part = jnp.sum(point_weights, axis=1)

    inv_c = inverse_norm(centroids)
    scores = jnp.einsum("pd,kd->pk", points, centroids, preferred_element_type=jnp.float32)
    expo = jnp.exp(scores * inv_x[:, None] * inv_c[None, :] * (1.0 / (width * TAU)))
    row_part = None
    for step in range(ITERS):
        if step == 0:
            col_part = jnp.sum(expo, axis=0)
        else:
            col_part = jnp.sum(expo * row_scale[:, None], axis=0)
        col_scale = 1.0 / dp_sum(col_part)
        row_part = jnp.sum(expo * col_scale[None, :], axis=1)
        if step + 1 < ITERS:
            row_scale = 1.0 / cent_sum(row_part)

    row_total = cent_sum(row_part)
    denominator = cent_sum(denom_part)
    row_scale = 1.0 / row_total
    assign = (expo * row_scale[:, None] * col_scale[None, :] * total_cent).astype(jnp.bfloat16)
    sub_assign = (total_sub * point_weights / denominator[:, None]).astype(jnp.bfloat16)
    return (assign, sub_assign)


def solution(mesh):
    return jax.shard_map(
        shards,
        mesh=mesh,
        in_specs=(P("dp", None), P("dp", None), P("cent", None), P("dp", "cent", None)),
        out_specs=(P("dp", "cent"), P("dp", "cent")),
        check_vma=False,
    )
```

```python
import jax
import jax.numpy as jnp
from jax import lax
from jax.sharding import PartitionSpec as P

CAP = 64
ITERS = 3


EPS = 1e-06
TAU = 0.05


def inverse_norm(rows):
    values = rows.astype(jnp.float32)
    return lax.rsqrt(jnp.mean(values * values, axis=-1) + EPS)


def shift_pairs(count, stride, size, step):
    pairs = []
    for i in range(count):
        digit = (i // stride) % size
        pairs.append((i, i + (((digit + step) % size) - digit) * stride))
    return pairs


def dp_sum(values):
    count = lax.axis_size("dp")
    for stride, size in ((1, 2), (2, 4), (8, count // 8)):
        if size < 2:
            continue
        parts = [lax.ppermute(values, "dp", shift_pairs(count, stride, size, step)) for step in range(1, size)]
        for part in parts:
            values = values + part
    return values


def cent_sum(values):
    count = lax.axis_size("cent")
    bit = 1
    while bit < count:
        values = values + lax.ppermute(values, "cent", [(i, i ^ bit) for i in range(count)])
        bit *= 2
    return values


def shards(points, cluster_ids, centroids, sub_centroids):
    pts_count = points.shape[0]
    width = points.shape[1]
    dp_count = lax.axis_size("dp")
    cent_count = lax.axis_size("cent")
    group_dev = sub_centroids.shape[0]
    sub_dev = sub_centroids.shape[1]
    clusters = group_dev * dp_count
    total_cent = centroids.shape[0] * cent_count
    total_sub = sub_dev * cent_count
    scale_two = 1.0 / (width * TAU)

    own_inv = inverse_norm(sub_centroids)
    spread = own_inv * 65537.0
    high = spread - (spread - own_inv)
    rest = own_inv - high
    spread = rest * 65537.0
    mid = spread - (spread - rest)
    low = (rest - mid).astype(jnp.bfloat16)
    high = high.astype(jnp.bfloat16)
    mid = mid.astype(jnp.bfloat16)
    extra = jnp.concatenate([high, mid, low, jnp.zeros((group_dev, width - 3 * sub_dev), jnp.bfloat16)], axis=1)
    pad = jnp.zeros((group_dev, 7, width), jnp.bfloat16)
    packed = jnp.concatenate([sub_centroids, extra[:, None, :], pad], axis=1)
    arrived = lax.all_gather(packed, "dp", axis=0, tiled=True)
    gathered = arrived[:, :sub_dev, :]
    parts = arrived[:, sub_dev, : 3 * sub_dev].astype(jnp.float32)
    inv_u = (parts[:, :sub_dev] + parts[:, sub_dev : 2 * sub_dev]) + parts[:, 2 * sub_dev :]
    inv_x = inverse_norm(points)
    ids = cluster_ids[:, 0]
    labels = lax.broadcasted_iota(jnp.int32, (pts_count, clusters), 1)
    onehot = ids[:, None] == labels
    positions = lax.broadcasted_iota(jnp.int32, (pts_count, pts_count), 0)
    earlier = (positions > positions.T).astype(jnp.bfloat16)
    before = jnp.dot(earlier, onehot.astype(jnp.bfloat16), preferred_element_type=jnp.float32)
    rank = jnp.sum(before * onehot.astype(jnp.float32), axis=1).astype(jnp.int32)
    slot = ids * CAP + rank
    source = jnp.zeros((clusters * CAP,), jnp.int32).at[slot].set(jnp.arange(pts_count, dtype=jnp.int32))
    pick = (source[:, None] == lax.broadcasted_iota(jnp.int32, (clusters * CAP, pts_count), 1)).astype(points.dtype)
    buffer = jnp.dot(pick, points, preferred_element_type=jnp.float32).astype(points.dtype)
    buffer = buffer.reshape(clusters, CAP, width)
    inv_rows = inverse_norm(buffer)
    dots = jnp.einsum("gcd,gkd->gck", buffer, gathered, preferred_element_type=jnp.float32)
    weights = jnp.exp(dots * inv_rows[..., None] * inv_u[:, None, :] * scale_two)
    point_weights = weights.reshape(clusters * CAP, sub_dev)[slot]
    denom_part = jnp.sum(point_weights, axis=1)

    inv_c = inverse_norm(centroids)
    scores = jnp.einsum("pd,kd->pk", points, centroids, preferred_element_type=jnp.float32)
    expo = jnp.exp(scores * inv_x[:, None] * inv_c[None, :] * (1.0 / (width * TAU)))
    row_part = None
    for step in range(ITERS):
        if step == 0:
            col_part = jnp.sum(expo, axis=0)
        else:
            col_part = jnp.sum(expo * row_scale[:, None], axis=0)
        col_scale = 1.0 / dp_sum(col_part)
        row_part = jnp.sum(expo * col_scale[None, :], axis=1)
        if step + 1 < ITERS:
            row_scale = 1.0 / lax.psum(row_part, "cent")

    row_total = cent_sum(row_part)
    denominator = cent_sum(denom_part)
    row_scale = 1.0 / row_total
    assign = (expo * row_scale[:, None] * col_scale[None, :] * total_cent).astype(jnp.bfloat16)
    sub_assign = (total_sub * point_weights / denominator[:, None]).astype(jnp.bfloat16)
    return (assign, sub_assign)


def solution(mesh):
    return jax.shard_map(
        shards,
        mesh=mesh,
        in_specs=(P("dp", None), P("dp", None), P("cent", None), P("dp", "cent", None)),
        out_specs=(P("dp", "cent"), P("dp", "cent")),
        check_vma=False,
    )
```

```python
import jax
import jax.numpy as jnp
from jax import lax
from jax.sharding import PartitionSpec as P

CAP = 64
ITERS = 3


EPS = 1e-06
TAU = 0.05


def inverse_norm(rows):
    values = rows.astype(jnp.float32)
    return lax.rsqrt(jnp.mean(values * values, axis=-1) + EPS)


def shift_pairs(count, stride, size, step):
    pairs = []
    for i in range(count):
        digit = (i // stride) % size
        pairs.append((i, i + (((digit + step) % size) - digit) * stride))
    return pairs


def dp_sum(values):
    count = lax.axis_size("dp")
    for stride, size in ((1, 2), (2, 4), (8, count // 8)):
        if size < 2:
            continue
        parts = [lax.ppermute(values, "dp", shift_pairs(count, stride, size, step)) for step in range(1, size)]
        for part in parts:
            values = values + part
    return values


def cent_sum(values):
    count = lax.axis_size("cent")
    values = values + lax.ppermute(values, "cent", [(i, i ^ 1) for i in range(count)])
    parts = [lax.ppermute(values, "cent", shift_pairs(count, 1, count, step)) for step in range(2, count, 2)]
    for part in parts:
        values = values + part
    return values


def shards(points, cluster_ids, centroids, sub_centroids):
    pts_count = points.shape[0]
    width = points.shape[1]
    dp_count = lax.axis_size("dp")
    cent_count = lax.axis_size("cent")
    group_dev = sub_centroids.shape[0]
    sub_dev = sub_centroids.shape[1]
    clusters = group_dev * dp_count
    total_cent = centroids.shape[0] * cent_count
    total_sub = sub_dev * cent_count
    scale_two = 1.0 / (width * TAU)

    own_inv = inverse_norm(sub_centroids)
    spread = own_inv * 65537.0
    high = spread - (spread - own_inv)
    rest = own_inv - high
    spread = rest * 65537.0
    mid = spread - (spread - rest)
    low = (rest - mid).astype(jnp.bfloat16)
    high = high.astype(jnp.bfloat16)
    mid = mid.astype(jnp.bfloat16)
    extra = jnp.concatenate([high, mid, low, jnp.zeros((group_dev, width - 3 * sub_dev), jnp.bfloat16)], axis=1)
    pad = jnp.zeros((group_dev, 7, width), jnp.bfloat16)
    packed = jnp.concatenate([sub_centroids, extra[:, None, :], pad], axis=1)
    arrived = lax.all_gather(packed, "dp", axis=0, tiled=True)
    gathered = arrived[:, :sub_dev, :]
    parts = arrived[:, sub_dev, : 3 * sub_dev].astype(jnp.float32)
    inv_u = (parts[:, :sub_dev] + parts[:, sub_dev : 2 * sub_dev]) + parts[:, 2 * sub_dev :]
    inv_x = inverse_norm(points)
    ids = cluster_ids[:, 0]
    labels = lax.broadcasted_iota(jnp.int32, (pts_count, clusters), 1)
    onehot = ids[:, None] == labels
    positions = lax.broadcasted_iota(jnp.int32, (pts_count, pts_count), 0)
    earlier = (positions > positions.T).astype(jnp.bfloat16)
    before = jnp.dot(earlier, onehot.astype(jnp.bfloat16), preferred_element_type=jnp.float32)
    rank = jnp.sum(before * onehot.astype(jnp.float32), axis=1).astype(jnp.int32)
    slot = ids * CAP + rank
    source = jnp.zeros((clusters * CAP,), jnp.int32).at[slot].set(jnp.arange(pts_count, dtype=jnp.int32))
    pick = (source[:, None] == lax.broadcasted_iota(jnp.int32, (clusters * CAP, pts_count), 1)).astype(points.dtype)
    buffer = jnp.dot(pick, points, preferred_element_type=jnp.float32).astype(points.dtype)
    buffer = buffer.reshape(clusters, CAP, width)
    inv_rows = inverse_norm(buffer)
    dots = jnp.einsum("gcd,gkd->gck", buffer, gathered, preferred_element_type=jnp.float32)
    weights = jnp.exp(dots * inv_rows[..., None] * inv_u[:, None, :] * scale_two)
    point_weights = weights.reshape(clusters * CAP, sub_dev)[slot]
    denom_part = jnp.sum(point_weights, axis=1)

    inv_c = inverse_norm(centroids)
    scores = jnp.einsum("pd,kd->pk", points, centroids, preferred_element_type=jnp.float32)
    expo = jnp.exp(scores * inv_x[:, None] * inv_c[None, :] * (1.0 / (width * TAU)))
    row_part = None
    for step in range(ITERS):
        if step == 0:
            col_part = jnp.sum(expo, axis=0)
        else:
            col_part = jnp.sum(expo * row_scale[:, None], axis=0)
        col_scale = 1.0 / dp_sum(col_part)
        row_part = jnp.sum(expo * col_scale[None, :], axis=1)
        if step + 1 < ITERS:
            row_scale = 1.0 / cent_sum(row_part)

    row_total = cent_sum(row_part)
    denominator = cent_sum(denom_part)
    row_scale = 1.0 / row_total
    assign = (expo * row_scale[:, None] * col_scale[None, :] * total_cent).astype(jnp.bfloat16)
    sub_assign = (total_sub * point_weights / denominator[:, None]).astype(jnp.bfloat16)
    return (assign, sub_assign)


def solution(mesh):
    return jax.shard_map(
        shards,
        mesh=mesh,
        in_specs=(P("dp", None), P("dp", None), P("cent", None), P("dp", "cent", None)),
        out_specs=(P("dp", "cent"), P("dp", "cent")),
        check_vma=False,
    )
```

```python
import jax
import jax.numpy as jnp
from jax import lax
from jax.sharding import PartitionSpec as P

CAP = 64
ITERS = 3


EPS = 1e-06
TAU = 0.05


def inverse_norm(rows):
    values = rows.astype(jnp.float32)
    return lax.rsqrt(jnp.mean(values * values, axis=-1) + EPS)


def shift_pairs(count, stride, size, step):
    pairs = []
    for i in range(count):
        digit = (i // stride) % size
        pairs.append((i, i + (((digit + step) % size) - digit) * stride))
    return pairs


def dp_sum(values):
    count = lax.axis_size("dp")
    for stride, size in ((1, 2), (2, 4), (8, count // 8)):
        if size < 2:
            continue
        parts = [lax.ppermute(values, "dp", shift_pairs(count, stride, size, step)) for step in range(1, size)]
        for part in parts:
            values = values + part
    return values


def cent_sum(values):
    count = lax.axis_size("cent")
    bit = 1
    while bit < count:
        values = values + lax.ppermute(values, "cent", [(i, i ^ bit) for i in range(count)])
        bit *= 2
    return values


def shards(points, cluster_ids, centroids, sub_centroids):
    pts_count = points.shape[0]
    width = points.shape[1]
    dp_count = lax.axis_size("dp")
    cent_count = lax.axis_size("cent")
    group_dev = sub_centroids.shape[0]
    sub_dev = sub_centroids.shape[1]
    clusters = group_dev * dp_count
    total_cent = centroids.shape[0] * cent_count
    total_sub = sub_dev * cent_count
    scale_two = 1.0 / (width * TAU)

    own_inv = inverse_norm(sub_centroids)
    spread = own_inv * 65537.0
    high = spread - (spread - own_inv)
    rest = own_inv - high
    spread = rest * 65537.0
    mid = spread - (spread - rest)
    low = (rest - mid).astype(jnp.bfloat16)
    high = high.astype(jnp.bfloat16)
    mid = mid.astype(jnp.bfloat16)
    extra = jnp.concatenate([high, mid, low, jnp.zeros((group_dev, width - 3 * sub_dev), jnp.bfloat16)], axis=1)
    pad = jnp.zeros((group_dev, 7, width), jnp.bfloat16)
    packed = jnp.concatenate([sub_centroids, extra[:, None, :], pad], axis=1)
    arrived = lax.all_gather(packed, "dp", axis=0, tiled=True)
    gathered = arrived[:, :sub_dev, :]
    parts = arrived[:, sub_dev, : 3 * sub_dev].astype(jnp.float32)
    inv_u = (parts[:, :sub_dev] + parts[:, sub_dev : 2 * sub_dev]) + parts[:, 2 * sub_dev :]
    inv_x = inverse_norm(points)
    ids = cluster_ids[:, 0]
    labels = lax.broadcasted_iota(jnp.int32, (pts_count, clusters), 1)
    onehot = ids[:, None] == labels
    positions = lax.broadcasted_iota(jnp.int32, (pts_count, pts_count), 0)
    earlier = (positions > positions.T).astype(jnp.bfloat16)
    before = jnp.dot(earlier, onehot.astype(jnp.bfloat16), preferred_element_type=jnp.float32)
    rank = jnp.sum(before * onehot.astype(jnp.float32), axis=1).astype(jnp.int32)
    slot = ids * CAP + rank
    pick = (slot[None, :] == lax.broadcasted_iota(jnp.int32, (clusters * CAP, pts_count), 0)).astype(points.dtype)
    buffer = jnp.dot(pick, points, preferred_element_type=jnp.float32).astype(points.dtype)
    buffer = buffer.reshape(clusters, CAP, width)
    inv_rows = inverse_norm(buffer)
    dots = jnp.einsum("gcd,gkd->gck", buffer, gathered, preferred_element_type=jnp.float32)
    weights = jnp.exp(dots * inv_rows[..., None] * inv_u[:, None, :] * scale_two)
    point_weights = weights.reshape(clusters * CAP, sub_dev)[slot]
    denom_part = jnp.sum(point_weights, axis=1)

    inv_c = inverse_norm(centroids)
    scores = jnp.einsum("pd,kd->pk", points, centroids, preferred_element_type=jnp.float32)
    expo = jnp.exp(scores * inv_x[:, None] * inv_c[None, :] * (1.0 / (width * TAU)))
    row_part = None
    for step in range(ITERS):
        if step == 0:
            col_part = jnp.sum(expo, axis=0)
        else:
            col_part = jnp.sum(expo * row_scale[:, None], axis=0)
        col_scale = 1.0 / dp_sum(col_part)
        row_part = jnp.sum(expo * col_scale[None, :], axis=1)
        if step + 1 < ITERS:
            row_scale = 1.0 / cent_sum(row_part)

    row_total = cent_sum(row_part)
    denominator = cent_sum(denom_part)
    row_scale = 1.0 / row_total
    assign = (expo * row_scale[:, None] * col_scale[None, :] * total_cent).astype(jnp.bfloat16)
    sub_assign = (total_sub * point_weights / denominator[:, None]).astype(jnp.bfloat16)
    return (assign, sub_assign)


def solution(mesh):
    return jax.shard_map(
        shards,
        mesh=mesh,
        in_specs=(P("dp", None), P("dp", None), P("cent", None), P("dp", "cent", None)),
        out_specs=(P("dp", "cent"), P("dp", "cent")),
        check_vma=False,
    )
```

```python
import jax
import jax.numpy as jnp
from jax import lax
from jax.sharding import PartitionSpec as P

CAP = 64
ITERS = 3


EPS = 1e-06
TAU = 0.05


def inverse_norm(rows):
    values = rows.astype(jnp.float32)
    return lax.rsqrt(jnp.mean(values * values, axis=-1) + EPS)


def shift_pairs(count, stride, size, step):
    pairs = []
    for i in range(count):
        digit = (i // stride) % size
        pairs.append((i, i + (((digit + step) % size) - digit) * stride))
    return pairs


def dp_sum(values):
    count = lax.axis_size("dp")
    for stride, size in ((1, 2), (2, 4), (8, count // 8)):
        if size < 2:
            continue
        parts = [lax.ppermute(values, "dp", shift_pairs(count, stride, size, step)) for step in range(1, size)]
        for part in parts:
            values = values + part
    return values


def cent_sum(values):
    count = lax.axis_size("cent")
    bit = 1
    while bit < count:
        values = values + lax.ppermute(values, "cent", [(i, i ^ bit) for i in range(count)])
        bit *= 2
    return values


def shards(points, cluster_ids, centroids, sub_centroids):
    pts_count = points.shape[0]
    width = points.shape[1]
    dp_count = lax.axis_size("dp")
    cent_count = lax.axis_size("cent")
    group_dev = sub_centroids.shape[0]
    sub_dev = sub_centroids.shape[1]
    clusters = group_dev * dp_count
    total_cent = centroids.shape[0] * cent_count
    total_sub = sub_dev * cent_count
    scale_two = 1.0 / (width * TAU)

    own_inv = inverse_norm(sub_centroids)
    spread = own_inv * 65537.0
    high = spread - (spread - own_inv)
    rest = own_inv - high
    spread = rest * 65537.0
    mid = spread - (spread - rest)
    low = (rest - mid).astype(jnp.bfloat16)
    high = high.astype(jnp.bfloat16)
    mid = mid.astype(jnp.bfloat16)
    extra = jnp.concatenate([high, mid, low, jnp.zeros((group_dev, width - 3 * sub_dev), jnp.bfloat16)], axis=1)
    pad = jnp.zeros((group_dev, 7, width), jnp.bfloat16)
    packed = jnp.concatenate([sub_centroids, extra[:, None, :], pad], axis=1)
    arrived = lax.all_gather(packed, "dp", axis=0, tiled=True)
    gathered = arrived[:, :sub_dev, :]
    parts = arrived[:, sub_dev, : 3 * sub_dev].astype(jnp.float32)
    inv_u = (parts[:, :sub_dev] + parts[:, sub_dev : 2 * sub_dev]) + parts[:, 2 * sub_dev :]
    inv_x = inverse_norm(points)
    ids = cluster_ids[:, 0]
    labels = lax.broadcasted_iota(jnp.int32, (pts_count, clusters), 1)
    onehot = ids[:, None] == labels
    positions = lax.broadcasted_iota(jnp.int32, (pts_count, pts_count), 0)
    earlier = (positions > positions.T).astype(jnp.bfloat16)
    before = jnp.dot(earlier, onehot.astype(jnp.bfloat16), preferred_element_type=jnp.float32)
    rank = jnp.sum(before * onehot.astype(jnp.float32), axis=1).astype(jnp.int32)
    slot = ids * CAP + rank
    chunks = 4
    per_chunk = clusters // chunks
    pieces = []
    for chunk in range(chunks):
        first = chunk * per_chunk * CAP
        rows = lax.broadcasted_iota(jnp.int32, (per_chunk * CAP, pts_count), 0) + first
        pick = (slot[None, :] == rows).astype(points.dtype)
        buffer = jnp.dot(pick, points, preferred_element_type=jnp.float32).astype(points.dtype)
        buffer = buffer.reshape(per_chunk, CAP, width)
        inv_rows = inverse_norm(buffer)
        own_subs = gathered[chunk * per_chunk : (chunk + 1) * per_chunk]
        own_inv_u = inv_u[chunk * per_chunk : (chunk + 1) * per_chunk]
        dots = jnp.einsum("gcd,gkd->gck", buffer, own_subs, preferred_element_type=jnp.float32)
        pieces.append(jnp.exp(dots * inv_rows[..., None] * own_inv_u[:, None, :] * scale_two))
    weights = jnp.concatenate(pieces, axis=0)
    point_weights = weights.reshape(clusters * CAP, sub_dev)[slot]
    denom_part = jnp.sum(point_weights, axis=1)

    inv_c = inverse_norm(centroids)
    scores = jnp.einsum("pd,kd->pk", points, centroids, preferred_element_type=jnp.float32)
    expo = jnp.exp(scores * inv_x[:, None] * inv_c[None, :] * (1.0 / (width * TAU)))
    row_part = None
    for step in range(ITERS):
        if step == 0:
            col_part = jnp.sum(expo, axis=0)
        else:
            col_part = jnp.sum(expo * row_scale[:, None], axis=0)
        col_scale = 1.0 / dp_sum(col_part)
        row_part = jnp.sum(expo * col_scale[None, :], axis=1)
        if step + 1 < ITERS:
            row_scale = 1.0 / cent_sum(row_part)

    row_total = cent_sum(row_part)
    denominator = cent_sum(denom_part)
    row_scale = 1.0 / row_total
    assign = (expo * row_scale[:, None] * col_scale[None, :] * total_cent).astype(jnp.bfloat16)
    sub_assign = (total_sub * point_weights / denominator[:, None]).astype(jnp.bfloat16)
    return (assign, sub_assign)


def solution(mesh):
    return jax.shard_map(
        shards,
        mesh=mesh,
        in_specs=(P("dp", None), P("dp", None), P("cent", None), P("dp", "cent", None)),
        out_specs=(P("dp", "cent"), P("dp", "cent")),
        check_vma=False,
    )
```

```python
import jax
import jax.numpy as jnp
from jax import lax
from jax.sharding import PartitionSpec as P

CAP = 64
ITERS = 3


EPS = 1e-06
TAU = 0.05


def inverse_norm(rows):
    values = rows.astype(jnp.float32)
    return lax.rsqrt(jnp.mean(values * values, axis=-1) + EPS)


def shift_pairs(count, stride, size, step):
    pairs = []
    for i in range(count):
        digit = (i // stride) % size
        pairs.append((i, i + (((digit + step) % size) - digit) * stride))
    return pairs


def dp_sum(values):
    count = lax.axis_size("dp")
    for stride, size in ((1, 2), (2, 4), (8, count // 8)):
        if size < 2:
            continue
        parts = [lax.ppermute(values, "dp", shift_pairs(count, stride, size, step)) for step in range(1, size)]
        for part in parts:
            values = values + part
    return values


def cent_sum(values):
    count = lax.axis_size("cent")
    bit = 1
    while bit < count:
        values = values + lax.ppermute(values, "cent", [(i, i ^ bit) for i in range(count)])
        bit *= 2
    return values


def shards(points, cluster_ids, centroids, sub_centroids):
    pts_count = points.shape[0]
    width = points.shape[1]
    dp_count = lax.axis_size("dp")
    cent_count = lax.axis_size("cent")
    group_dev = sub_centroids.shape[0]
    sub_dev = sub_centroids.shape[1]
    clusters = group_dev * dp_count
    total_cent = centroids.shape[0] * cent_count
    total_sub = sub_dev * cent_count
    scale_two = 1.0 / (width * TAU)

    own_inv = inverse_norm(sub_centroids)
    spread = own_inv * 65537.0
    high = spread - (spread - own_inv)
    rest = own_inv - high
    spread = rest * 65537.0
    mid = spread - (spread - rest)
    low = (rest - mid).astype(jnp.bfloat16)
    high = high.astype(jnp.bfloat16)
    mid = mid.astype(jnp.bfloat16)
    extra = jnp.concatenate([high, mid, low, jnp.zeros((group_dev, width - 3 * sub_dev), jnp.bfloat16)], axis=1)
    pad = jnp.zeros((group_dev, 7, width), jnp.bfloat16)
    packed = jnp.concatenate([sub_centroids, extra[:, None, :], pad], axis=1)
    arrived = lax.all_gather(packed, "dp", axis=0, tiled=True)
    gathered = arrived[:, :sub_dev, :]
    parts = arrived[:, sub_dev, : 3 * sub_dev].astype(jnp.float32)
    inv_u = (parts[:, :sub_dev] + parts[:, sub_dev : 2 * sub_dev]) + parts[:, 2 * sub_dev :]
    inv_x = inverse_norm(points)
    ids = cluster_ids[:, 0]
    labels = lax.broadcasted_iota(jnp.int32, (pts_count, clusters), 1)
    onehot = ids[:, None] == labels
    positions = lax.broadcasted_iota(jnp.int32, (pts_count, pts_count), 0)
    earlier = (positions > positions.T).astype(jnp.bfloat16)
    before = jnp.dot(earlier, onehot.astype(jnp.bfloat16), preferred_element_type=jnp.float32)
    rank = jnp.sum(before * onehot.astype(jnp.float32), axis=1).astype(jnp.int32)
    slot = ids * CAP + rank
    pick = (slot[None, :] == lax.broadcasted_iota(jnp.int32, (clusters * CAP, pts_count), 0)).astype(points.dtype)
    buffer = jnp.dot(pick, points, preferred_element_type=jnp.float32).astype(points.dtype)
    buffer = buffer.reshape(clusters, CAP, width)
    inv_rows = inverse_norm(buffer)
    dots = jnp.einsum("gcd,gkd->gck", buffer, gathered, preferred_element_type=jnp.float32)
    weights = jnp.exp(dots * inv_rows[..., None] * inv_u[:, None, :] * scale_two)
    slot_weights = weights.reshape(clusters * CAP, sub_dev)
    denom_part = jnp.sum(slot_weights, axis=1)[slot]
    point_weights = slot_weights[slot]

    inv_c = inverse_norm(centroids)
    scores = jnp.einsum("pd,kd->pk", points, centroids, preferred_element_type=jnp.float32)
    expo = jnp.exp(scores * inv_x[:, None] * inv_c[None, :] * (1.0 / (width * TAU)))
    row_part = None
    for step in range(ITERS):
        if step == 0:
            col_part = jnp.sum(expo, axis=0)
        else:
            col_part = jnp.sum(expo * row_scale[:, None], axis=0)
        col_scale = 1.0 / dp_sum(col_part)
        row_part = jnp.sum(expo * col_scale[None, :], axis=1)
        if step + 1 < ITERS:
            row_scale = 1.0 / cent_sum(row_part)

    row_total = cent_sum(row_part)
    denominator = cent_sum(denom_part)
    row_scale = 1.0 / row_total
    assign = (expo * row_scale[:, None] * col_scale[None, :] * total_cent).astype(jnp.bfloat16)
    sub_assign = (total_sub * point_weights / denominator[:, None]).astype(jnp.bfloat16)
    return (assign, sub_assign)


def solution(mesh):
    return jax.shard_map(
        shards,
        mesh=mesh,
        in_specs=(P("dp", None), P("dp", None), P("cent", None), P("dp", "cent", None)),
        out_specs=(P("dp", "cent"), P("dp", "cent")),
        check_vma=False,
    )
```

```python
import jax
import jax.numpy as jnp
from jax import lax
from jax.sharding import PartitionSpec as P

CAP = 64
ITERS = 3


EPS = 1e-06
TAU = 0.05


def inverse_norm(rows):
    values = rows.astype(jnp.float32)
    return lax.rsqrt(jnp.mean(values * values, axis=-1) + EPS)


def shift_pairs(count, stride, size, step):
    pairs = []
    for i in range(count):
        digit = (i // stride) % size
        pairs.append((i, i + (((digit + step) % size) - digit) * stride))
    return pairs


def dp_sum(values):
    count = lax.axis_size("dp")
    for stride, size in ((1, 2), (2, 4), (8, count // 8)):
        if size < 2:
            continue
        parts = [lax.ppermute(values, "dp", shift_pairs(count, stride, size, step)) for step in range(1, size)]
        for part in parts:
            values = values + part
    return values


def cent_sum(values):
    count = lax.axis_size("cent")
    bit = 1
    while bit < count:
        values = values + lax.ppermute(values, "cent", [(i, i ^ bit) for i in range(count)])
        bit *= 2
    return values


def shards(points, cluster_ids, centroids, sub_centroids):
    pts_count = points.shape[0]
    width = points.shape[1]
    dp_count = lax.axis_size("dp")
    cent_count = lax.axis_size("cent")
    group_dev = sub_centroids.shape[0]
    sub_dev = sub_centroids.shape[1]
    clusters = group_dev * dp_count
    total_cent = centroids.shape[0] * cent_count
    total_sub = sub_dev * cent_count
    scale_two = 1.0 / (width * TAU)

    own_inv = inverse_norm(sub_centroids)
    spread = own_inv * 65537.0
    high = spread - (spread - own_inv)
    rest = own_inv - high
    spread = rest * 65537.0
    mid = spread - (spread - rest)
    low = (rest - mid).astype(jnp.bfloat16)
    high = high.astype(jnp.bfloat16)
    mid = mid.astype(jnp.bfloat16)
    extra = jnp.concatenate([high, mid, low, jnp.zeros((group_dev, width - 3 * sub_dev), jnp.bfloat16)], axis=1)
    pad = jnp.zeros((group_dev, 7, width), jnp.bfloat16)
    packed = jnp.concatenate([sub_centroids, extra[:, None, :], pad], axis=1)
    arrived = lax.all_gather(packed, "dp", axis=0, tiled=True)
    gathered = arrived[:, :sub_dev, :]
    parts = arrived[:, sub_dev, : 3 * sub_dev].astype(jnp.float32)
    inv_u = (parts[:, :sub_dev] + parts[:, sub_dev : 2 * sub_dev]) + parts[:, 2 * sub_dev :]
    inv_x = inverse_norm(points)
    ids = cluster_ids[:, 0]
    labels = lax.broadcasted_iota(jnp.int32, (pts_count, clusters), 1)
    onehot = ids[:, None] == labels
    positions = lax.broadcasted_iota(jnp.int32, (pts_count, pts_count), 0)
    earlier = (positions > positions.T).astype(jnp.bfloat16)
    before = jnp.dot(earlier, onehot.astype(jnp.bfloat16), preferred_element_type=jnp.float32)
    rank = jnp.sum(before * onehot.astype(jnp.float32), axis=1).astype(jnp.int32)
    slot = ids * CAP + rank
    pick = (slot[None, :] == lax.broadcasted_iota(jnp.int32, (clusters * CAP, pts_count), 0)).astype(points.dtype)
    buffer = jnp.dot(pick, points, preferred_element_type=jnp.float32).astype(points.dtype)
    buffer = buffer.reshape(clusters, CAP, width)
    inv_rows = inverse_norm(buffer)
    dots = jnp.einsum("gcd,gkd->gck", buffer, gathered, preferred_element_type=jnp.float32)
    weights = jnp.exp(dots * inv_rows[..., None] * inv_u[:, None, :] * scale_two)
    point_weights = weights.reshape(clusters * CAP, sub_dev)[slot]
    denom_part = jnp.sum(point_weights, axis=1)

    inv_c = inverse_norm(centroids)
    scores = jnp.einsum("pd,kd->pk", points, centroids, preferred_element_type=jnp.float32)
    expo = jnp.exp(scores * inv_x[:, None] * inv_c[None, :] * (1.0 / (width * TAU)))
    row_part = None
    for step in range(ITERS):
        if step == 0:
            col_part = jnp.sum(expo, axis=0)
        else:
            col_part = jnp.sum(expo * row_scale[:, None], axis=0)
        col_scale = 1.0 / dp_sum(col_part)
        row_part = jnp.sum(expo * col_scale[None, :], axis=1)
        if step + 1 < ITERS:
            row_scale = 1.0 / cent_sum(row_part)

    row_part, denom_part = lax.optimization_barrier((row_part, denom_part))
    row_total = cent_sum(row_part)
    denominator = cent_sum(denom_part)
    row_scale = 1.0 / row_total
    assign = (expo * row_scale[:, None] * col_scale[None, :] * total_cent).astype(jnp.bfloat16)
    sub_assign = (total_sub * point_weights / denominator[:, None]).astype(jnp.bfloat16)
    return (assign, sub_assign)


def solution(mesh):
    return jax.shard_map(
        shards,
        mesh=mesh,
        in_specs=(P("dp", None), P("dp", None), P("cent", None), P("dp", "cent", None)),
        out_specs=(P("dp", "cent"), P("dp", "cent")),
        check_vma=False,
    )
```

```python
import jax
import jax.numpy as jnp
from jax import lax
from jax.sharding import PartitionSpec as P

CAP = 64
ITERS = 3


EPS = 1e-06
TAU = 0.05


def inverse_norm(rows):
    values = rows.astype(jnp.float32)
    return lax.rsqrt(jnp.mean(values * values, axis=-1) + EPS)


def shift_pairs(count, stride, size, step):
    pairs = []
    for i in range(count):
        digit = (i // stride) % size
        pairs.append((i, i + (((digit + step) % size) - digit) * stride))
    return pairs


def dp_sum(values):
    count = lax.axis_size("dp")
    for stride, size in ((1, 2), (2, 4), (8, count // 8)):
        if size < 2:
            continue
        parts = [lax.ppermute(values, "dp", shift_pairs(count, stride, size, step)) for step in range(1, size)]
        for part in parts:
            values = values + part
    return values


def cent_sum(values):
    count = lax.axis_size("cent")
    bit = 1
    while bit < count:
        values = values + lax.ppermute(values, "cent", [(i, i ^ bit) for i in range(count)])
        bit *= 2
    return values


def shards(points, cluster_ids, centroids, sub_centroids):
    pts_count = points.shape[0]
    width = points.shape[1]
    dp_count = lax.axis_size("dp")
    cent_count = lax.axis_size("cent")
    group_dev = sub_centroids.shape[0]
    sub_dev = sub_centroids.shape[1]
    clusters = group_dev * dp_count
    total_cent = centroids.shape[0] * cent_count
    total_sub = sub_dev * cent_count
    scale_two = 1.0 / (width * TAU)

    own_inv = inverse_norm(sub_centroids)
    spread = own_inv * 65537.0
    high = spread - (spread - own_inv)
    rest = own_inv - high
    spread = rest * 65537.0
    mid = spread - (spread - rest)
    low = (rest - mid).astype(jnp.bfloat16)
    high = high.astype(jnp.bfloat16)
    mid = mid.astype(jnp.bfloat16)
    extra = jnp.concatenate([high, mid, low, jnp.zeros((group_dev, width - 3 * sub_dev), jnp.bfloat16)], axis=1)
    pad = jnp.zeros((group_dev, 7, width), jnp.bfloat16)
    packed = jnp.concatenate([sub_centroids, extra[:, None, :], pad], axis=1)
    arrived = lax.all_gather(packed, "dp", axis=0, tiled=True)
    gathered = arrived[:, :sub_dev, :]
    parts = arrived[:, sub_dev, : 3 * sub_dev].astype(jnp.float32)
    inv_u = (parts[:, :sub_dev] + parts[:, sub_dev : 2 * sub_dev]) + parts[:, 2 * sub_dev :]
    inv_x = inverse_norm(points)
    ids = cluster_ids[:, 0]
    labels = lax.broadcasted_iota(jnp.int32, (pts_count, clusters), 1)
    onehot = ids[:, None] == labels
    positions = lax.broadcasted_iota(jnp.int32, (pts_count, pts_count), 0)
    earlier = (positions > positions.T).astype(jnp.bfloat16)
    before = jnp.dot(earlier, onehot.astype(jnp.bfloat16), preferred_element_type=jnp.float32)
    rank = jnp.sum(before * onehot.astype(jnp.float32), axis=1).astype(jnp.int32)
    slot = ids * CAP + rank
    pick = (slot[None, :] == lax.broadcasted_iota(jnp.int32, (clusters * CAP, pts_count), 0)).astype(points.dtype)
    buffer = jnp.dot(pick, points, preferred_element_type=jnp.float32).astype(points.dtype)
    buffer = buffer.reshape(clusters, CAP, width)
    inv_rows = inverse_norm(buffer)
    dots = jnp.einsum("gcd,gkd->gck", buffer, gathered, preferred_element_type=jnp.float32)
    weights = jnp.exp(dots * inv_rows[..., None] * inv_u[:, None, :] * scale_two)
    slot_weights = weights.reshape(clusters * CAP, sub_dev)
    denom_part = jnp.sum(slot_weights, axis=1)[slot]
    point_weights = slot_weights[slot]

    inv_c = inverse_norm(centroids)
    scores = jnp.einsum("pd,kd->pk", points, centroids, preferred_element_type=jnp.float32)
    expo = jnp.exp(scores * inv_x[:, None] * inv_c[None, :] * (1.0 / (width * TAU)))
    row_part = None
    for step in range(ITERS):
        if step == 0:
            col_part = jnp.sum(expo, axis=0)
        else:
            col_part = jnp.sum(expo * row_scale[:, None], axis=0)
        col_scale = 1.0 / dp_sum(col_part)
        row_part = jnp.sum(expo * col_scale[None, :], axis=1)
        if step + 1 < ITERS:
            row_scale = 1.0 / cent_sum(row_part)

    row_part, denom_part = lax.optimization_barrier((row_part, denom_part))
    row_total = cent_sum(row_part)
    denominator = cent_sum(denom_part)
    row_scale = 1.0 / row_total
    assign = (expo * row_scale[:, None] * col_scale[None, :] * total_cent).astype(jnp.bfloat16)
    sub_assign = (total_sub * point_weights / denominator[:, None]).astype(jnp.bfloat16)
    return (assign, sub_assign)


def solution(mesh):
    return jax.shard_map(
        shards,
        mesh=mesh,
        in_specs=(P("dp", None), P("dp", None), P("cent", None), P("dp", "cent", None)),
        out_specs=(P("dp", "cent"), P("dp", "cent")),
        check_vma=False,
    )
```
